256 devices in a mesh: wave: 8 (over z_hi, x), region: 32 (over z_lo, y, core).
Axes of the slice: x: 4, y: 4, z: 8 (z_hi: 2, z_lo: 4; z = z_hi * 4 + z_lo), core: 2. Of those that a mesh axis runs over, the one named last changes fastest.
Arguments:
- object_field: float32 [2, 16384, 1024], P(None, 'region'), may hold values from -5 to 5
- probes: float32 [8, 2, 256, 256], P('wave'), may hold values from -5 to 5
- patterns: bfloat16 [8, 512, 256, 256], P('wave', 'region'), may hold values from 0 to 2
- offsets: int32 [512, 2], P('region'), may hold values from 0 to 768, as said below
- counts: int32 [32], P('region'), may hold values from 1 to 16, as said below
Outputs:
- object_grad: float32 [2, 16384, 1024], P(None, 'region', 'wave')
- probe_grad: float32 [8, 2, 256, 256], P('wave')
The draws below stay inside these ranges and needn't reach their ends.
Inputs may be any that keep to these rules, and one draw needn't show every extreme that they name: Offsets are whole cells: row offsets below 512, column offsets at most 768. `counts`: some tile uses all slots and some tile uses one.
All inputs are finite; a program needn't handle non-finite values.
Results may differ from the reference program's by a relative error of at most 0.0052.
Values sent between devices are 32-bit elements; how exact they have to be, the bound alone decides.
No kernel may reach another device: no remote copies, remote signals or barrier semaphores. Data moves between devices by JAX's collectives and lax.ppermute only.
A program may use at most 128 MiB of HBM per device.

```python
import math
import jax
import jax.numpy as jnp
from jax import lax

PATCH = 256
TILE = 512
WIDTH = 1024
POS = 16
WAVES = 8
ROWS = 16384
POSITIONS = 512


def draw_offsets(key, part):
    first_key, second_key = jax.random.split(jax.random.fold_in(key, 11))
    row_vals = jax.random.randint(first_key, (POSITIONS,), 0, TILE, dtype=jnp.int32)
    col_vals = jax.random.randint(second_key, (POSITIONS,), 0, WIDTH - PATCH + 1, dtype=jnp.int32)
    row_vals = row_vals.at[0].set(TILE - 1).at[1].set(0)
    col_vals = col_vals.at[2].set(WIDTH - PATCH).at[3].set(0)
    return jnp.stack([row_vals, col_vals], axis=1).astype(jnp.int32)


def draw_counts(key, part):
    first_key, second_key = jax.random.split(jax.random.fold_in(key, 23))
    tiles = POSITIONS // POS
    base_vals = jax.random.randint(first_key, (tiles,), 1, POS + 1, dtype=jnp.int32)
    order = jax.random.permutation(second_key, tiles)
    base_vals = base_vals.at[order[0]].set(POS).at[order[1]].set(1)
    return base_vals.astype(jnp.int32)


def steps_of(rng, shape, cuts, least, largest):
    level = 1.0
    for dim, parts in cuts:
        draws = jax.random.uniform(jax.random.fold_in(jax.random.fold_in(rng, 6), dim), (parts,), jnp.float32, least / len(cuts), largest / len(cuts))
        level = level * jnp.repeat(jnp.exp(draws), shape[dim] // parts).reshape((-1,) + (1,) * (len(shape) - 1 - dim))
    return level


def scatter_about(stream_key, dims, spread, reach, pieces=(), kind=jnp.bfloat16):
    values = jax.random.normal(stream_key, dims, jnp.float32) * spread
    if len(pieces) > 0:
        values = steps_of(stream_key, dims, pieces, -0.22, 0.18) * values
    return jnp.clip(values, min=-reach, max=reach).astype(kind)


def setup_inputs(seed: int = 0) -> dict:
    streams_of = jax.random.split(jax.random.key(seed), 6)
    object_field = scatter_about(streams_of[0], (2, ROWS, WIDTH), 0.7, 5.0, ((1, 32),), jnp.float32)
    probes = scatter_about(streams_of[1], (WAVES, 2, PATCH, PATCH), 0.7, 5.0, ((0, 8),), jnp.float32)
    patterns = jnp.clip(2.0 * jax.random.uniform(streams_of[2], (WAVES, POSITIONS, PATCH, PATCH), jnp.float32) ** steps_of(streams_of[2], (WAVES, POSITIONS, PATCH, PATCH), ((0, 8), (1, 32)), -0.2, 0.2), 0.0, 2.0).astype(jnp.bfloat16)
    offsets = draw_offsets(jax.random.fold_in(streams_of[5], 71), 0)
    counts = draw_counts(jax.random.fold_in(streams_of[5], 71), 0)
    return dict(object_field=object_field, probes=probes, patterns=patterns, offsets=offsets, counts=counts)


def make_tables():
    index = jnp.arange(PATCH, dtype=jnp.int32)
    phase_int = index[:, None] * index[None, :] % PATCH
    phase = phase_int.astype(jnp.float32) * (2.0 * math.pi / PATCH)
    scale = 1.0 / math.sqrt(PATCH)
    cos_table = (jnp.cos(phase) * scale).astype(jnp.bfloat16).astype(jnp.float32)
    sin_table = (jnp.sin(phase) * scale).astype(jnp.bfloat16).astype(jnp.float32)
    return (cos_table, sin_table)

def to_grid(value):
    return lax.optimization_barrier(value.astype(jnp.bfloat16)).astype(jnp.float32)

def apply_left(table, field_part):
    return jnp.einsum('kn,wnm->wkm', table, field_part)

def apply_right(field_part, table):
    return jnp.einsum('wkn,nm->wkm', field_part, table)

def reference(object_field, probes, patterns, offsets, counts):
    cos_table, sin_table = make_tables()
    padded = jnp.concatenate([object_field, jnp.zeros((2, PATCH, WIDTH), jnp.float32)], axis=1)
    probe_re = probes[:, 0]
    probe_im = probes[:, 1]

    def advance(state_pair, slot):
        grad_ext, probe_acc = state_pair
        tile_index = slot // POS
        slot_index = slot % POS
        row_at = (tile_index * TILE + offsets[slot, 0]).astype(jnp.int32)
        col_at = offsets[slot, 1].astype(jnp.int32)
        zero_at = jnp.zeros((), jnp.int32)
        patch_cut = lax.dynamic_slice(padded, (zero_at, row_at, col_at), (2, PATCH, PATCH))
        wave_re = to_grid(probe_re * patch_cut[0] - probe_im * patch_cut[1])
        wave_im = to_grid(probe_re * patch_cut[1] + probe_im * patch_cut[0])
        half_re = to_grid(apply_left(cos_table, wave_re) + apply_left(sin_table, wave_im))
        half_im = to_grid(apply_left(cos_table, wave_im) - apply_left(sin_table, wave_re))
        far_re = apply_right(half_re, cos_table) + apply_right(half_im, sin_table)
        far_im = apply_right(half_im, cos_table) - apply_right(half_re, sin_table)
        measured = lax.dynamic_index_in_dim(patterns, slot, 1, keepdims=False).astype(jnp.float32)
        excess = far_re * far_re + far_im * far_im - measured
        back_re = to_grid(excess * far_re)
        back_im = to_grid(excess * far_im)
        inner_re = to_grid(apply_left(cos_table, back_re) - apply_left(sin_table, back_im))
        inner_im = to_grid(apply_left(cos_table, back_im) + apply_left(sin_table, back_re))
        chi_re = apply_right(inner_re, cos_table) - apply_right(inner_im, sin_table)
        chi_im = apply_right(inner_im, cos_table) + apply_right(inner_re, sin_table)
        in_use = (slot_index < counts[tile_index]).astype(jnp.float32)
        obj_re = lax.optimization_barrier(jnp.sum(probe_re * chi_re + probe_im * chi_im, axis=0)) * in_use
        obj_im = lax.optimization_barrier(jnp.sum(probe_re * chi_im - probe_im * chi_re, axis=0)) * in_use
        current = lax.dynamic_slice(grad_ext, (zero_at, row_at, col_at), (2, PATCH, PATCH))
        grad_ext = lax.dynamic_update_slice(grad_ext, current + jnp.stack([obj_re, obj_im]), (zero_at, row_at, col_at))
        prb_re = (patch_cut[0] * chi_re + patch_cut[1] * chi_im) * in_use
        prb_im = (patch_cut[0] * chi_im - patch_cut[1] * chi_re) * in_use
        probe_acc = probe_acc + jnp.stack([prb_re, prb_im], axis=1)
        return ((grad_ext, probe_acc), None)
    start_state = (jnp.zeros((2, ROWS + PATCH, WIDTH), jnp.float32), jnp.zeros((WAVES, 2, PATCH, PATCH), jnp.float32))
    (grad_ext, probe_acc), _ = lax.scan(advance, start_state, jnp.arange(POSITIONS, dtype=jnp.int32))
    return (grad_ext[:, :ROWS], probe_acc)
```

```python
import math

import jax
import jax.numpy as jnp
from jax import lax
from jax.experimental import pallas as pl
from jax.experimental.pallas import tpu as pltpu
from jax.sharding import PartitionSpec as P

SUB = 8
LANE = 128


def from_behind(block, axis, distance):
    devices = range(lax.axis_size(axis))
    route = [(i - distance, i) for i in devices if i - distance in devices]
    return lax.ppermute(block, axis, route)


def xor_route(axis, bit):
    return [(i, i ^ (1 << bit)) for i in range(lax.axis_size(axis))]


def sum_over(block, axis):
    for bit in range(lax.axis_size(axis).bit_length() - 1):
        block = block + lax.ppermute(block, axis, xor_route(axis, bit))
    return block


def sum_scatter_columns(block, axis):
    count = lax.axis_size(axis)
    bits = count.bit_length() - 1
    me = lax.axis_index(axis)
    lead = block.shape[:-1]
    width = block.shape[-1] // count
    held = block.reshape(lead + (2,) * bits + (width,))
    for bit in range(bits):
        place = len(lead) + bits - 1 - bit
        mine = (me >> bit) & 1
        kept = lax.dynamic_index_in_dim(held, mine, place, keepdims=False)
        sent = lax.dynamic_index_in_dim(held, 1 - mine, place, keepdims=False)
        held = kept + lax.ppermute(sent, axis, xor_route(axis, bit))
    return held


def windows(offsets, patch_side, width_cols):
    rows = offsets[:, 0]
    cols = offsets[:, 1]
    base = (rows // SUB) * SUB
    down = rows - base
    start = jnp.minimum((cols // LANE) * LANE, width_cols - patch_side - LANE)
    shift = cols - start
    return base, down, start, shift


def extract_kernel(base_ref, down_ref, start_ref, shift_ref, ext_ref, out_ref):
    s = pl.program_id(0)
    side = out_ref.shape[-1]
    high = side + SUB
    wide = side + LANE
    base = pl.multiple_of(base_ref[s], SUB)
    start = pl.multiple_of(start_ref[s], LANE)
    up = (high - down_ref[s]) % high
    left = (wide - shift_ref[s]) % wide
    for c in range(2):
        win = ext_ref[c, pl.ds(base, high), pl.ds(start, wide)]
        win = pltpu.roll(win, up, 0)
        win = pltpu.roll(win, left, 1)
        out_ref[0, c] = win[:side, :side]


def extract_patches(extended, base, down, start, shift, patch_side):
    slots = base.shape[0]
    grid_spec = pltpu.PrefetchScalarGridSpec(
        num_scalar_prefetch=4,
        grid=(slots,),
        in_specs=[pl.BlockSpec(extended.shape, lambda s, *_: (0, 0, 0))],
        out_specs=pl.BlockSpec((1, 2, patch_side, patch_side), lambda s, *_: (s, 0, 0, 0)),
    )
    return pl.pallas_call(
        extract_kernel,
        grid_spec=grid_spec,
        out_shape=jax.ShapeDtypeStruct((slots, 2, patch_side, patch_side), jnp.float32),
        compiler_params=pltpu.CompilerParams(vmem_limit_bytes=48 * 1024 * 1024),
    )(base, down, start, shift, extended)


def accumulate_kernel(base_ref, down_ref, start_ref, shift_ref, count_ref, terms_ref, out_ref, pad_ref):
    s = pl.program_id(0)
    side = terms_ref.shape[-1]
    high = side + SUB
    wide = side + LANE

    @pl.when(s == 0)
    def _():
        out_ref[...] = jnp.zeros_like(out_ref)
        pad_ref[...] = jnp.zeros_like(pad_ref)

    @pl.when(s < count_ref[0])
    def _():
        base = pl.multiple_of(base_ref[s], SUB)
        start = pl.multiple_of(start_ref[s], LANE)
        down = down_ref[s]
        shift = shift_ref[s]
        for c in range(2):
            pad_ref[:side, :side] = terms_ref[0, c]
            term = pltpu.roll(pad_ref[...], down, 0)
            term = pltpu.roll(term, shift, 1)
            out_ref[c, pl.ds(base, high), pl.ds(start, wide)] += term


def accumulate_terms(terms, base, down, start, shift, count, rows_out, width_cols):
    slots, _, side, _ = terms.shape
    grid_spec = pltpu.PrefetchScalarGridSpec(
        num_scalar_prefetch=5,
        grid=(slots,),
        in_specs=[pl.BlockSpec((1, 2, side, side), lambda s, *_: (s, 0, 0, 0))],
        out_specs=pl.BlockSpec((2, rows_out, width_cols), lambda s, *_: (0, 0, 0)),
        scratch_shapes=[pltpu.VMEM((side + SUB, side + LANE), jnp.float32)],
    )
    return pl.pallas_call(
        accumulate_kernel,
        grid_spec=grid_spec,
        out_shape=jax.ShapeDtypeStruct((2, rows_out, width_cols), jnp.float32),
        compiler_params=pltpu.CompilerParams(vmem_limit_bytes=48 * 1024 * 1024),
    )(base, down, start, shift, count, terms)


def make_tables(patch_side):
    index = jnp.arange(patch_side, dtype=jnp.int32)
    phase_int = index[:, None] * index[None, :] % patch_side
    phase = phase_int.astype(jnp.float32) * (2.0 * math.pi / patch_side)
    scale = 1.0 / math.sqrt(patch_side)
    return (
        (jnp.cos(phase) * scale).astype(jnp.bfloat16),
        (jnp.sin(phase) * scale).astype(jnp.bfloat16),
    )


def apply_left(table, field_part):
    return jnp.einsum("kn,bnm->bkm", table, field_part, preferred_element_type=jnp.float32)


def apply_right(field_part, table):
    return jnp.einsum("bkn,nm->bkm", field_part, table, preferred_element_type=jnp.float32)


def on_device(object_field, probes, patterns, offsets, counts):
    tile_rows = object_field.shape[1]
    width_cols = object_field.shape[2]
    patch_side = probes.shape[-1]
    slot_total = offsets.shape[0]
    top_rows = object_field[:, :patch_side, :]
    rim_rows = from_behind(top_rows, "region", -1)
    extended = jnp.concatenate([object_field, rim_rows], axis=1)
    base, down, start, shift = windows(offsets, patch_side, width_cols)
    patches = extract_patches(extended, base, down, start, shift, patch_side)
    cos_table, sin_table = make_tables(patch_side)
    probe_re = probes[0, 0]
    probe_im = probes[0, 1]
    wave_re = (probe_re * patches[:, 0] - probe_im * patches[:, 1]).astype(jnp.bfloat16)
    wave_im = (probe_re * patches[:, 1] + probe_im * patches[:, 0]).astype(jnp.bfloat16)
    half_re = (apply_left(cos_table, wave_re) + apply_left(sin_table, wave_im)).astype(jnp.bfloat16)
    half_im = (apply_left(cos_table, wave_im) - apply_left(sin_table, wave_re)).astype(jnp.bfloat16)
    far_re = apply_right(half_re, cos_table) + apply_right(half_im, sin_table)
    far_im = apply_right(half_im, cos_table) - apply_right(half_re, sin_table)
    excess = far_re * far_re + far_im * far_im - patterns[0].astype(jnp.float32)
    back_re = (excess * far_re).astype(jnp.bfloat16)
    back_im = (excess * far_im).astype(jnp.bfloat16)
    inner_re = (apply_left(cos_table, back_re) - apply_left(sin_table, back_im)).astype(
        jnp.bfloat16
    )
    inner_im = (apply_left(cos_table, back_im) + apply_left(sin_table, back_re)).astype(
        jnp.bfloat16
    )
    chi_re = apply_right(inner_re, cos_table) - apply_right(inner_im, sin_table)
    chi_im = apply_right(inner_im, cos_table) + apply_right(inner_re, sin_table)
    in_use = (jnp.arange(slot_total, dtype=jnp.int32) < counts[0]).astype(jnp.float32)[
        :, None, None
    ]
    obj_terms = jnp.stack(
        [
            (probe_re * chi_re + probe_im * chi_im) * in_use,
            (probe_re * chi_im - probe_im * chi_re) * in_use,
        ],
        axis=1,
    )
    prb_re = jnp.sum((patches[:, 0] * chi_re + patches[:, 1] * chi_im) * in_use, axis=0)
    prb_im = jnp.sum((patches[:, 0] * chi_im - patches[:, 1] * chi_re) * in_use, axis=0)
    probe_total = sum_over(jnp.stack([prb_re, prb_im]), "region")

    grad_ext = accumulate_terms(
        obj_terms, base, down, start, shift, counts, tile_rows + patch_side, width_cols
    )
    arrived = from_behind(grad_ext[:, tile_rows:, :], "region", 1)
    tile_grad = grad_ext[:, :tile_rows, :] + jnp.pad(
        arrived, ((0, 0), (0, tile_rows - patch_side), (0, 0))
    )
    object_out = sum_scatter_columns(tile_grad, "wave")
    return (object_out, probe_total[None])


def solution(mesh):
    in_specs = (
        P(None, "region", None),
        P("wave", None, None, None),
        P("wave", "region", None, None),
        P("region", None),
        P("region"),
    )
    out_specs = (P(None, "region", "wave"), P("wave", None, None, None))
    return jax.shard_map(
        on_device, mesh=mesh, in_specs=in_specs, out_specs=out_specs, check_vma=False
    )
```

```python
import math

import jax
import jax.numpy as jnp
from jax import lax
from jax.experimental import pallas as pl
from jax.experimental.pallas import tpu as pltpu
from jax.sharding import PartitionSpec as P

SUB = 8
LANE = 128


def from_behind(block, axis, distance):
    devices = range(lax.axis_size(axis))
    route = [(i - distance, i) for i in devices if i - distance in devices]
    return lax.ppermute(block, axis, route)


def xor_route(axis, bit):
    return [(i, i ^ (1 << bit)) for i in range(lax.axis_size(axis))]


def sum_over(block, axis):
    for bit in range(lax.axis_size(axis).bit_length() - 1):
        block = block + lax.ppermute(block, axis, xor_route(axis, bit))
    return block


def sum_scatter_blocks(held, axis):
    bits = lax.axis_size(axis).bit_length() - 1
    held = held.reshape((2,) * bits + held.shape[1:])
    for bit in range(bits):
        place = bits - 1 - bit
        kept = lax.index_in_dim(held, 0, place, keepdims=False)
        sent = lax.index_in_dim(held, 1, place, keepdims=False)
        held = kept + lax.ppermute(sent, axis, xor_route(axis, bit))
    return held


def windows(offsets, patch_side, width_cols):
    rows = offsets[:, 0]
    cols = offsets[:, 1]
    base = (rows // SUB) * SUB
    down = rows - base
    start = jnp.minimum((cols // LANE) * LANE, width_cols - patch_side - LANE)
    shift = cols - start
    return base, down, start, shift


def extract_kernel(base_ref, down_ref, start_ref, shift_ref, ext_ref, out_ref):
    s = pl.program_id(0)
    side = out_ref.shape[-1]
    high = side + SUB
    wide = side + LANE
    base = pl.multiple_of(base_ref[s], SUB)
    start = pl.multiple_of(start_ref[s], LANE)
    up = (high - down_ref[s]) % high
    left = (wide - shift_ref[s]) % wide
    for c in range(2):
        win = ext_ref[c, pl.ds(base, high), pl.ds(start, wide)]
        win = pltpu.roll(win, up, 0)
        win = pltpu.roll(win, left, 1)
        out_ref[0, c] = win[:side, :side]


def extract_patches(extended, base, down, start, shift, patch_side):
    slots = base.shape[0]
    grid_spec = pltpu.PrefetchScalarGridSpec(
        num_scalar_prefetch=4,
        grid=(slots,),
        in_specs=[pl.BlockSpec(extended.shape, lambda s, *_: (0, 0, 0))],
        out_specs=pl.BlockSpec((1, 2, patch_side, patch_side), lambda s, *_: (s, 0, 0, 0)),
    )
    return pl.pallas_call(
        extract_kernel,
        grid_spec=grid_spec,
        out_shape=jax.ShapeDtypeStruct((slots, 2, patch_side, patch_side), jnp.float32),
        compiler_params=pltpu.CompilerParams(vmem_limit_bytes=48 * 1024 * 1024),
    )(base, down, start, shift, extended)


def accumulate_kernel(base_ref, down_ref, shift_ref, place_ref, count_ref, terms_ref, out_ref, pad_ref):
    s = pl.program_id(0)
    side = terms_ref.shape[-1]
    high = side + SUB
    spans = place_ref.shape[1]

    @pl.when(s == 0)
    def _():
        out_ref[...] = jnp.zeros_like(out_ref)
        pad_ref[...] = jnp.zeros_like(pad_ref)

    @pl.when(s < count_ref[0])
    def _():
        base = pl.multiple_of(base_ref[s], SUB)
        down = down_ref[s]
        shift = shift_ref[s]
        for c in range(2):
            pad_ref[:side, :side] = terms_ref[0, c]
            term = pltpu.roll(pad_ref[...], down, 0)
            term = pltpu.roll(term, shift, 1)
            for k in range(spans):
                out_ref[place_ref[s, k], c, pl.ds(base, high), :] += term[:, k * LANE:(k + 1) * LANE]


def accumulate_terms(terms, base, down, shift, place, count, blocks, rows_out):
    slots, _, side, _ = terms.shape
    grid_spec = pltpu.PrefetchScalarGridSpec(
        num_scalar_prefetch=5,
        grid=(slots,),
        in_specs=[pl.BlockSpec((1, 2, side, side), lambda s, *_: (s, 0, 0, 0))],
        out_specs=pl.BlockSpec((blocks, 2, rows_out, LANE), lambda s, *_: (0, 0, 0, 0)),
        scratch_shapes=[pltpu.VMEM((side + SUB, side + LANE), jnp.float32)],
    )
    return pl.pallas_call(
        accumulate_kernel,
        grid_spec=grid_spec,
        out_shape=jax.ShapeDtypeStruct((blocks, 2, rows_out, LANE), jnp.float32),
        compiler_params=pltpu.CompilerParams(vmem_limit_bytes=48 * 1024 * 1024),
    )(base, down, shift, place, count, terms)


def make_tables(patch_side):
    index = jnp.arange(patch_side, dtype=jnp.int32)
    phase_int = index[:, None] * index[None, :] % patch_side
    phase = phase_int.astype(jnp.float32) * (2.0 * math.pi / patch_side)
    scale = 1.0 / math.sqrt(patch_side)
    return (
        (jnp.cos(phase) * scale).astype(jnp.bfloat16),
        (jnp.sin(phase) * scale).astype(jnp.bfloat16),
    )


def apply_left(table, field_part):
    return jnp.einsum("kn,bnm->bkm", table, field_part, preferred_element_type=jnp.float32)


def apply_right(field_part, table):
    return jnp.einsum("bkn,nm->bkm", field_part, table, preferred_element_type=jnp.float32)


def on_device(object_field, probes, patterns, offsets, counts):
    tile_rows = object_field.shape[1]
    width_cols = object_field.shape[2]
    patch_side = probes.shape[-1]
    slot_total = offsets.shape[0]
    top_rows = object_field[:, :patch_side, :]
    rim_rows = from_behind(top_rows, "region", -1)
    extended = jnp.concatenate([object_field, rim_rows], axis=1)
    base, down, start, shift = windows(offsets, patch_side, width_cols)
    patches = extract_patches(extended, base, down, start, shift, patch_side)
    cos_table, sin_table = make_tables(patch_side)
    probe_re = probes[0, 0]
    probe_im = probes[0, 1]
    wave_re = (probe_re * patches[:, 0] - probe_im * patches[:, 1]).astype(jnp.bfloat16)
    wave_im = (probe_re * patches[:, 1] + probe_im * patches[:, 0]).astype(jnp.bfloat16)
    half_re = (apply_left(cos_table, wave_re) + apply_left(sin_table, wave_im)).astype(jnp.bfloat16)
    half_im = (apply_left(cos_table, wave_im) - apply_left(sin_table, wave_re)).astype(jnp.bfloat16)
    far_re = apply_right(half_re, cos_table) + apply_right(half_im, sin_table)
    far_im = apply_right(half_im, cos_table) - apply_right(half_re, sin_table)
    excess = far_re * far_re + far_im * far_im - patterns[0].astype(jnp.float32)
    back_re = (excess * far_re).astype(jnp.bfloat16)
    back_im = (excess * far_im).astype(jnp.bfloat16)
    inner_re = (apply_left(cos_table, back_re) - apply_left(sin_table, back_im)).astype(
        jnp.bfloat16
    )
    inner_im = (apply_left(cos_table, back_im) + apply_left(sin_table, back_re)).astype(
        jnp.bfloat16
    )
    chi_re = apply_right(inner_re, cos_table) - apply_right(inner_im, sin_table)
    chi_im = apply_right(inner_im, cos_table) + apply_right(inner_re, sin_table)
    in_use = (jnp.arange(slot_total, dtype=jnp.int32) < counts[0]).astype(jnp.float32)[
        :, None, None
    ]
    obj_terms = jnp.stack(
        [
            (probe_re * chi_re + probe_im * chi_im) * in_use,
            (probe_re * chi_im - probe_im * chi_re) * in_use,
        ],
        axis=1,
    )
    prb_re = jnp.sum((patches[:, 0] * chi_re + patches[:, 1] * chi_im) * in_use, axis=0)
    prb_im = jnp.sum((patches[:, 0] * chi_im - patches[:, 1] * chi_re) * in_use, axis=0)
    probe_total = sum_over(jnp.stack([prb_re, prb_im]), "region")

    blocks = lax.axis_size("wave")
    spans = (patch_side + LANE) // LANE
    first = start // LANE
    place = jnp.bitwise_xor(
        first[:, None] + jnp.arange(spans, dtype=jnp.int32)[None, :], lax.axis_index("wave")
    ).astype(jnp.int32)
    grad_ext = accumulate_terms(
        obj_terms, base, down, shift, place, counts, blocks, tile_rows + patch_side
    )
    arrived = from_behind(grad_ext[:, :, tile_rows:, :], "region", 1)
    tile_grad = grad_ext[:, :, :tile_rows, :] + jnp.pad(
        arrived, ((0, 0), (0, 0), (0, tile_rows - patch_side), (0, 0))
    )
    object_out = sum_scatter_blocks(tile_grad, "wave")
    return (object_out, probe_total[None])


def solution(mesh):
    in_specs = (
        P(None, "region", None),
        P("wave", None, None, None),
        P("wave", "region", None, None),
        P("region", None),
        P("region"),
    )
    out_specs = (P(None, "region", "wave"), P("wave", None, None, None))
    return jax.shard_map(
        on_device, mesh=mesh, in_specs=in_specs, out_specs=out_specs, check_vma=False
    )
```

```python
import math

import jax
import jax.numpy as jnp
from jax import lax
from jax.experimental import pallas as pl
from jax.experimental.pallas import tpu as pltpu
from jax.sharding import PartitionSpec as P

SUB = 8
LANE = 128


def from_behind(block, axis, distance):
    devices = range(lax.axis_size(axis))
    route = [(i - distance, i) for i in devices if i - distance in devices]
    return lax.ppermute(block, axis, route)


def xor_route(axis, bit):
    return [(i, i ^ (1 << bit)) for i in range(lax.axis_size(axis))]


def sum_over(block, axis):
    for bit in range(lax.axis_size(axis).bit_length() - 1):
        block = block + lax.ppermute(block, axis, xor_route(axis, bit))
    return block


def sum_scatter_blocks(held, axis):
    bits = lax.axis_size(axis).bit_length() - 1
    held = held.reshape((2,) * bits + held.shape[1:])
    for bit in range(bits):
        place = bits - 1 - bit
        kept = lax.index_in_dim(held, 0, place, keepdims=False)
        sent = lax.index_in_dim(held, 1, place, keepdims=False)
        held = kept + lax.ppermute(sent, axis, xor_route(axis, bit))
    return held


def windows(offsets, patch_side, width_cols):
    rows = offsets[:, 0]
    cols = offsets[:, 1]
    base = (rows // SUB) * SUB
    down = rows - base
    start = jnp.minimum((cols // LANE) * LANE, width_cols - patch_side - LANE)
    shift = cols - start
    return base, down, start, shift


def extract_kernel(base_ref, down_ref, start_ref, shift_ref, ext_ref, out_ref):
    s = pl.program_id(0)
    side = out_ref.shape[-1]
    high = side + SUB
    wide = side + LANE
    base = pl.multiple_of(base_ref[s], SUB)
    start = pl.multiple_of(start_ref[s], LANE)
    up = (high - down_ref[s]) % high
    left = (wide - shift_ref[s]) % wide
    for c in range(2):
        win = ext_ref[c, pl.ds(base, high), pl.ds(start, wide)]
        win = pltpu.roll(win, up, 0)
        win = pltpu.roll(win, left, 1)
        out_ref[0, c] = win[:side, :side]


def extract_patches(extended, base, down, start, shift, patch_side):
    slots = base.shape[0]
    grid_spec = pltpu.PrefetchScalarGridSpec(
        num_scalar_prefetch=4,
        grid=(slots,),
        in_specs=[pl.BlockSpec(extended.shape, lambda s, *_: (0, 0, 0))],
        out_specs=pl.BlockSpec((1, 2, patch_side, patch_side), lambda s, *_: (s, 0, 0, 0)),
    )
    return pl.pallas_call(
        extract_kernel,
        grid_spec=grid_spec,
        out_shape=jax.ShapeDtypeStruct((slots, 2, patch_side, patch_side), jnp.float32),
        compiler_params=pltpu.CompilerParams(vmem_limit_bytes=48 * 1024 * 1024),
    )(base, down, start, shift, extended)


def accumulate_kernel(base_ref, down_ref, shift_ref, place_ref, count_ref, terms_ref, out_ref, pad_ref):
    s = pl.program_id(0)
    side = terms_ref.shape[-1]
    high = side + SUB
    spans = place_ref.shape[1]

    @pl.when(s == 0)
    def _():
        out_ref[...] = jnp.zeros_like(out_ref)
        pad_ref[...] = jnp.zeros_like(pad_ref)

    @pl.when(s < count_ref[0])
    def _():
        base = pl.multiple_of(base_ref[s], SUB)
        down = down_ref[s]
        shift = shift_ref[s]
        for c in range(2):
            pad_ref[:side, :side] = terms_ref[0, c]
            term = pltpu.roll(pad_ref[...], down, 0)
            term = pltpu.roll(term, shift, 1)
            for k in range(spans):
                out_ref[place_ref[s, k], c, pl.ds(base, high), :] += term[:, k * LANE:(k + 1) * LANE]


def accumulate_terms(terms, base, down, shift, place, count, blocks, rows_out):
    slots, _, side, _ = terms.shape
    grid_spec = pltpu.PrefetchScalarGridSpec(
        num_scalar_prefetch=5,
        grid=(slots,),
        in_specs=[pl.BlockSpec((1, 2, side, side), lambda s, *_: (s, 0, 0, 0))],
        out_specs=pl.BlockSpec((blocks, 2, rows_out, LANE), lambda s, *_: (0, 0, 0, 0)),
        scratch_shapes=[pltpu.VMEM((side + SUB, side + LANE), jnp.float32)],
    )
    return pl.pallas_call(
        accumulate_kernel,
        grid_spec=grid_spec,
        out_shape=jax.ShapeDtypeStruct((blocks, 2, rows_out, LANE), jnp.float32),
        compiler_params=pltpu.CompilerParams(vmem_limit_bytes=48 * 1024 * 1024),
    )(base, down, shift, place, count, terms)


def fused_kernel(base_ref, down_ref, start_ref, shift_ref, place_ref, count_ref,
                 ext_ref, probe_ref, pattern_ref, cos_ref, sin_ref, grad_ref, prb_ref, pad_ref):
    s = pl.program_id(0)
    side = probe_ref.shape[-1]
    high = side + SUB
    wide = side + LANE
    spans = place_ref.shape[1]

    @pl.when(s == 0)
    def _():
        grad_ref[...] = jnp.zeros_like(grad_ref)
        prb_ref[...] = jnp.zeros_like(prb_ref)
        pad_ref[...] = jnp.zeros_like(pad_ref)

    @pl.when(s < count_ref[0])
    def _():
        base = pl.multiple_of(base_ref[s], SUB)
        start = pl.multiple_of(start_ref[s], LANE)
        down = down_ref[s]
        shift = shift_ref[s]
        up = (high - down) % high
        left = (wide - shift) % wide
        cut = []
        for c in range(2):
            win = ext_ref[c, pl.ds(base, high), pl.ds(start, wide)]
            win = pltpu.roll(win, up, 0)
            win = pltpu.roll(win, left, 1)
            cut.append(win[:side, :side])
        x_re, x_im = cut
        p_re = probe_ref[0]
        p_im = probe_ref[1]
        cos_t = cos_ref[...]
        sin_t = sin_ref[...]

        def left_mul(table, part):
            return jnp.dot(table, part, preferred_element_type=jnp.float32)

        def right_mul(part, table):
            return jnp.dot(part, table, preferred_element_type=jnp.float32)

        wave_re = (p_re * x_re - p_im * x_im).astype(jnp.bfloat16)
        wave_im = (p_re * x_im + p_im * x_re).astype(jnp.bfloat16)
        half_re = (left_mul(cos_t, wave_re) + left_mul(sin_t, wave_im)).astype(jnp.bfloat16)
        half_im = (left_mul(cos_t, wave_im) - left_mul(sin_t, wave_re)).astype(jnp.bfloat16)
        far_re = right_mul(half_re, cos_t) + right_mul(half_im, sin_t)
        far_im = right_mul(half_im, cos_t) - right_mul(half_re, sin_t)
        excess = far_re * far_re + far_im * far_im - pattern_ref[0].astype(jnp.float32)
        back_re = (excess * far_re).astype(jnp.bfloat16)
        back_im = (excess * far_im).astype(jnp.bfloat16)
        inner_re = (left_mul(cos_t, back_re) - left_mul(sin_t, back_im)).astype(jnp.bfloat16)
        inner_im = (left_mul(cos_t, back_im) + left_mul(sin_t, back_re)).astype(jnp.bfloat16)
        chi_re = right_mul(inner_re, cos_t) - right_mul(inner_im, sin_t)
        chi_im = right_mul(inner_im, cos_t) + right_mul(inner_re, sin_t)
        prb_ref[0] += x_re * chi_re + x_im * chi_im
        prb_ref[1] += x_re * chi_im - x_im * chi_re
        terms = (p_re * chi_re + p_im * chi_im, p_re * chi_im - p_im * chi_re)
        for c in range(2):
            pad_ref[:side, :side] = terms[c]
            term = pltpu.roll(pad_ref[...], down, 0)
            term = pltpu.roll(term, shift, 1)
            for k in range(spans):
                grad_ref[place_ref[s, k], c, pl.ds(base, high), :] += term[:, k * LANE:(k + 1) * LANE]


def fused_step(extended, probe, patterns, cos_table, sin_table, base, down, start, shift, place,
               count, blocks, rows_out):
    slots, side, _ = patterns.shape
    whole2 = lambda s, *_: (0, 0)
    whole3 = lambda s, *_: (0, 0, 0)
    grid_spec = pltpu.PrefetchScalarGridSpec(
        num_scalar_prefetch=6,
        grid=(slots,),
        in_specs=[
            pl.BlockSpec(extended.shape, whole3),
            pl.BlockSpec(probe.shape, whole3),
            pl.BlockSpec((1, side, side), lambda s, *_: (s, 0, 0)),
            pl.BlockSpec(cos_table.shape, whole2),
            pl.BlockSpec(sin_table.shape, whole2),
        ],
        out_specs=[
            pl.BlockSpec((blocks, 2, rows_out, LANE), lambda s, *_: (0, 0, 0, 0)),
            pl.BlockSpec(probe.shape, whole3),
        ],
        scratch_shapes=[pltpu.VMEM((side + SUB, side + LANE), jnp.float32)],
    )
    return pl.pallas_call(
        fused_kernel,
        grid_spec=grid_spec,
        out_shape=(
            jax.ShapeDtypeStruct((blocks, 2, rows_out, LANE), jnp.float32),
            jax.ShapeDtypeStruct(probe.shape, jnp.float32),
        ),
        compiler_params=pltpu.CompilerParams(vmem_limit_bytes=60 * 1024 * 1024),
    )(base, down, start, shift, place, count, extended, probe, patterns, cos_table, sin_table)


def make_tables(patch_side):
    index = jnp.arange(patch_side, dtype=jnp.int32)
    phase_int = index[:, None] * index[None, :] % patch_side
    phase = phase_int.astype(jnp.float32) * (2.0 * math.pi / patch_side)
    scale = 1.0 / math.sqrt(patch_side)
    return (
        (jnp.cos(phase) * scale).astype(jnp.bfloat16),
        (jnp.sin(phase) * scale).astype(jnp.bfloat16),
    )


def apply_left(table, field_part):
    return jnp.einsum("kn,bnm->bkm", table, field_part, preferred_element_type=jnp.float32)


def apply_right(field_part, table):
    return jnp.einsum("bkn,nm->bkm", field_part, table, preferred_element_type=jnp.float32)


def on_device(object_field, probes, patterns, offsets, counts):
    tile_rows = object_field.shape[1]
    width_cols = object_field.shape[2]
    patch_side = probes.shape[-1]
    slot_total = offsets.shape[0]
    top_rows = object_field[:, :patch_side, :]
    rim_rows = from_behind(top_rows, "region", -1)
    extended = jnp.concatenate([object_field, rim_rows], axis=1)
    base, down, start, shift = windows(offsets, patch_side, width_cols)
    cos_table, sin_table = make_tables(patch_side)
    blocks = lax.axis_size("wave")
    spans = (patch_side + LANE) // LANE
    first = start // LANE
    place = jnp.bitwise_xor(
        first[:, None] + jnp.arange(spans, dtype=jnp.int32)[None, :], lax.axis_index("wave")
    ).astype(jnp.int32)
    grad_ext, probe_part = fused_step(
        extended, probes[0], patterns[0], cos_table, sin_table, base, down, start, shift, place,
        counts, blocks, tile_rows + patch_side,
    )
    probe_total = sum_over(probe_part, "region")
    arrived = from_behind(grad_ext[:, :, tile_rows:, :], "region", 1)
    tile_grad = grad_ext[:, :, :tile_rows, :] + jnp.pad(
        arrived, ((0, 0), (0, 0), (0, tile_rows - patch_side), (0, 0))
    )
    object_out = sum_scatter_blocks(tile_grad, "wave")
    return (object_out, probe_total[None])


def solution(mesh):
    in_specs = (
        P(None, "region", None),
        P("wave", None, None, None),
        P("wave", "region", None, None),
        P("region", None),
        P("region"),
    )
    out_specs = (P(None, "region", "wave"), P("wave", None, None, None))
    return jax.shard_map(
        on_device, mesh=mesh, in_specs=in_specs, out_specs=out_specs, check_vma=False
    )
```

```python
import math

import jax
import jax.numpy as jnp
from jax import lax
from jax.experimental import pallas as pl
from jax.experimental.pallas import tpu as pltpu
from jax.sharding import PartitionSpec as P

SUB = 8
LANE = 128


def from_behind(block, axis, distance):
    devices = range(lax.axis_size(axis))
    route = [(i - distance, i) for i in devices if i - distance in devices]
    return lax.ppermute(block, axis, route)


def xor_route(axis, bit):
    return [(i, i ^ (1 << bit)) for i in range(lax.axis_size(axis))]


def sum_over(block, axis, order):
    for bit in order:
        block = block + lax.ppermute(block, axis, xor_route(axis, bit))
    return block


def sum_scatter_blocks(held, axis):
    bits = lax.axis_size(axis).bit_length() - 1
    held = held.reshape((2,) * bits + held.shape[1:])
    for bit in range(bits):
        place = bits - 1 - bit
        kept = lax.index_in_dim(held, 0, place, keepdims=False)
        sent = lax.index_in_dim(held, 1, place, keepdims=False)
        held = kept + lax.ppermute(sent, axis, xor_route(axis, bit))
    return held


def windows(offsets, patch_side, width_cols):
    rows = offsets[:, 0]
    cols = offsets[:, 1]
    base = (rows // SUB) * SUB
    down = rows - base
    start = jnp.minimum((cols // LANE) * LANE, width_cols - patch_side - LANE)
    shift = cols - start
    return base, down, start, shift


def extract_kernel(base_ref, down_ref, start_ref, shift_ref, ext_ref, out_ref):
    s = pl.program_id(0)
    side = out_ref.shape[-1]
    high = side + SUB
    wide = side + LANE
    base = pl.multiple_of(base_ref[s], SUB)
    start = pl.multiple_of(start_ref[s], LANE)
    up = (high - down_ref[s]) % high
    left = (wide - shift_ref[s]) % wide
    for c in range(2):
        win = ext_ref[c, pl.ds(base, high), pl.ds(start, wide)]
        win = pltpu.roll(win, up, 0)
        win = pltpu.roll(win, left, 1)
        out_ref[0, c] = win[:side, :side]


def extract_patches(extended, base, down, start, shift, patch_side):
    slots = base.shape[0]
    grid_spec = pltpu.PrefetchScalarGridSpec(
        num_scalar_prefetch=4,
        grid=(slots,),
        in_specs=[pl.BlockSpec(extended.shape, lambda s, *_: (0, 0, 0))],
        out_specs=pl.BlockSpec((1, 2, patch_side, patch_side), lambda s, *_: (s, 0, 0, 0)),
    )
    return pl.pallas_call(
        extract_kernel,
        grid_spec=grid_spec,
        out_shape=jax.ShapeDtypeStruct((slots, 2, patch_side, patch_side), jnp.float32),
        compiler_params=pltpu.CompilerParams(vmem_limit_bytes=48 * 1024 * 1024),
    )(base, down, start, shift, extended)


def accumulate_kernel(base_ref, down_ref, shift_ref, place_ref, count_ref, terms_ref, out_ref, pad_ref):
    s = pl.program_id(0)
    side = terms_ref.shape[-1]
    high = side + SUB
    spans = place_ref.shape[1]

    @pl.when(s == 0)
    def _():
        out_ref[...] = jnp.zeros_like(out_ref)
        pad_ref[...] = jnp.zeros_like(pad_ref)

    @pl.when(s < count_ref[0])
    def _():
        base = pl.multiple_of(base_ref[s], SUB)
        down = down_ref[s]
        shift = shift_ref[s]
        for c in range(2):
            pad_ref[:side, :side] = terms_ref[0, c]
            term = pltpu.roll(pad_ref[...], down, 0)
            term = pltpu.roll(term, shift, 1)
            for k in range(spans):
                out_ref[place_ref[s, k], c, pl.ds(base, high), :] += term[:, k * LANE:(k + 1) * LANE]


def accumulate_terms(terms, base, down, shift, place, count, blocks, rows_out):
    slots, _, side, _ = terms.shape
    grid_spec = pltpu.PrefetchScalarGridSpec(
        num_scalar_prefetch=5,
        grid=(slots,),
        in_specs=[pl.BlockSpec((1, 2, side, side), lambda s, *_: (s, 0, 0, 0))],
        out_specs=pl.BlockSpec((blocks, 2, rows_out, LANE), lambda s, *_: (0, 0, 0, 0)),
        scratch_shapes=[pltpu.VMEM((side + SUB, side + LANE), jnp.float32)],
    )
    return pl.pallas_call(
        accumulate_kernel,
        grid_spec=grid_spec,
        out_shape=jax.ShapeDtypeStruct((blocks, 2, rows_out, LANE), jnp.float32),
        compiler_params=pltpu.CompilerParams(vmem_limit_bytes=48 * 1024 * 1024),
    )(base, down, shift, place, count, terms)


def fused_kernel(base_ref, down_ref, start_ref, shift_ref, place_ref, count_ref,
                 ext_ref, probe_ref, pattern_ref, cos_ref, sin_ref, grad_ref, prb_ref, pad_ref):
    s = pl.program_id(0)
    side = probe_ref.shape[-1]
    high = side + SUB
    wide = side + LANE
    spans = place_ref.shape[1]

    @pl.when(s == 0)
    def _():
        grad_ref[...] = jnp.zeros_like(grad_ref)
        prb_ref[...] = jnp.zeros_like(prb_ref)
        pad_ref[...] = jnp.zeros_like(pad_ref)

    @pl.when(s < count_ref[0])
    def _():
        base = pl.multiple_of(base_ref[s], SUB)
        start = pl.multiple_of(start_ref[s], LANE)
        down = down_ref[s]
        shift = shift_ref[s]
        up = (high - down) % high
        left = (wide - shift) % wide
        cut = []
        for c in range(2):
            win = ext_ref[c, pl.ds(base, high), pl.ds(start, wide)]
            win = pltpu.roll(win, up, 0)
            win = pltpu.roll(win, left, 1)
            cut.append(win[:side, :side])
        x_re, x_im = cut
        p_re = probe_ref[0]
        p_im = probe_ref[1]
        cos_t = cos_ref[...]
        sin_t = sin_ref[...]

        def left_mul(table, part):
            return jnp.dot(table, part, preferred_element_type=jnp.float32)

        def right_mul(part, table):
            return jnp.dot(part, table, preferred_element_type=jnp.float32)

        wave_re = (p_re * x_re - p_im * x_im).astype(jnp.bfloat16)
        wave_im = (p_re * x_im + p_im * x_re).astype(jnp.bfloat16)
        half_re = (left_mul(cos_t, wave_re) + left_mul(sin_t, wave_im)).astype(jnp.bfloat16)
        half_im = (left_mul(cos_t, wave_im) - left_mul(sin_t, wave_re)).astype(jnp.bfloat16)
        far_re = right_mul(half_re, cos_t) + right_mul(half_im, sin_t)
        far_im = right_mul(half_im, cos_t) - right_mul(half_re, sin_t)
        excess = far_re * far_re + far_im * far_im - pattern_ref[0].astype(jnp.float32)
        back_re = (excess * far_re).astype(jnp.bfloat16)
        back_im = (excess * far_im).astype(jnp.bfloat16)
        inner_re = (left_mul(cos_t, back_re) - left_mul(sin_t, back_im)).astype(jnp.bfloat16)
        inner_im = (left_mul(cos_t, back_im) + left_mul(sin_t, back_re)).astype(jnp.bfloat16)
        chi_re = right_mul(inner_re, cos_t) - right_mul(inner_im, sin_t)
        chi_im = right_mul(inner_im, cos_t) + right_mul(inner_re, sin_t)
        prb_ref[0] += x_re * chi_re + x_im * chi_im
        prb_ref[1] += x_re * chi_im - x_im * chi_re
        terms = (p_re * chi_re + p_im * chi_im, p_re * chi_im - p_im * chi_re)
        for c in range(2):
            pad_ref[:side, :side] = terms[c]
            term = pltpu.roll(pad_ref[...], down, 0)
            term = pltpu.roll(term, shift, 1)
            for k in range(spans):
                grad_ref[place_ref[s, k], c, pl.ds(base, high), :] += term[:, k * LANE:(k + 1) * LANE]


def fused_step(extended, probe, patterns, cos_table, sin_table, base, down, start, shift, place,
               count, blocks, rows_out):
    slots, side, _ = patterns.shape
    whole2 = lambda s, *_: (0, 0)
    whole3 = lambda s, *_: (0, 0, 0)
    grid_spec = pltpu.PrefetchScalarGridSpec(
        num_scalar_prefetch=6,
        grid=(slots,),
        in_specs=[
            pl.BlockSpec(extended.shape, whole3),
            pl.BlockSpec(probe.shape, whole3),
            pl.BlockSpec((1, side, side), lambda s, *_: (s, 0, 0)),
            pl.BlockSpec(cos_table.shape, whole2),
            pl.BlockSpec(sin_table.shape, whole2),
        ],
        out_specs=[
            pl.BlockSpec((blocks, 2, rows_out, LANE), lambda s, *_: (0, 0, 0, 0)),
            pl.BlockSpec(probe.shape, whole3),
        ],
        scratch_shapes=[pltpu.VMEM((side + SUB, side + LANE), jnp.float32)],
    )
    return pl.pallas_call(
        fused_kernel,
        grid_spec=grid_spec,
        out_shape=(
            jax.ShapeDtypeStruct((blocks, 2, rows_out, LANE), jnp.float32),
            jax.ShapeDtypeStruct(probe.shape, jnp.float32),
        ),
        compiler_params=pltpu.CompilerParams(vmem_limit_bytes=60 * 1024 * 1024),
    )(base, down, start, shift, place, count, extended, probe, patterns, cos_table, sin_table)


def make_tables(patch_side):
    index = jnp.arange(patch_side, dtype=jnp.int32)
    phase_int = index[:, None] * index[None, :] % patch_side
    phase = phase_int.astype(jnp.float32) * (2.0 * math.pi / patch_side)
    scale = 1.0 / math.sqrt(patch_side)
    return (
        (jnp.cos(phase) * scale).astype(jnp.bfloat16),
        (jnp.sin(phase) * scale).astype(jnp.bfloat16),
    )


def apply_left(table, field_part):
    return jnp.einsum("kn,bnm->bkm", table, field_part, preferred_element_type=jnp.float32)


def apply_right(field_part, table):
    return jnp.einsum("bkn,nm->bkm", field_part, table, preferred_element_type=jnp.float32)


def on_device(object_field, probes, patterns, offsets, counts):
    tile_rows = object_field.shape[1]
    width_cols = object_field.shape[2]
    patch_side = probes.shape[-1]
    slot_total = offsets.shape[0]
    top_rows = object_field[:, :patch_side, :]
    rim_rows = from_behind(top_rows, "region", -1)
    extended = jnp.concatenate([object_field, rim_rows], axis=1)
    base, down, start, shift = windows(offsets, patch_side, width_cols)
    cos_table, sin_table = make_tables(patch_side)
    blocks = lax.axis_size("wave")
    spans = (patch_side + LANE) // LANE
    first = start // LANE
    place = jnp.bitwise_xor(
        first[:, None] + jnp.arange(spans, dtype=jnp.int32)[None, :], lax.axis_index("wave")
    ).astype(jnp.int32)
    grad_ext, probe_part = fused_step(
        extended, probes[0], patterns[0], cos_table, sin_table, base, down, start, shift, place,
        counts, blocks, tile_rows + patch_side,
    )
    probe_total = sum_over(probe_part, "region", (3, 4, 0, 1, 2))
    arrived = from_behind(grad_ext[:, :, tile_rows:, :], "region", 1)
    lower_out = sum_scatter_blocks(grad_ext[:, :, patch_side:tile_rows, :], "wave")
    upper_out = sum_scatter_blocks(grad_ext[:, :, :patch_side, :] + arrived, "wave")
    object_out = jnp.concatenate([upper_out, lower_out], axis=1)
    return (object_out, probe_total[None])


def solution(mesh):
    in_specs = (
        P(None, "region", None),
        P("wave", None, None, None),
        P("wave", "region", None, None),
        P("region", None),
        P("region"),
    )
    out_specs = (P(None, "region", "wave"), P("wave", None, None, None))
    return jax.shard_map(
        on_device, mesh=mesh, in_specs=in_specs, out_specs=out_specs, check_vma=False
    )
```

```python
import math

import jax
import jax.numpy as jnp
from jax import lax
from jax.experimental import pallas as pl
from jax.experimental.pallas import tpu as pltpu
from jax.sharding import PartitionSpec as P

SUB = 8
LANE = 128


def from_behind(block, axis, distance):
    devices = range(lax.axis_size(axis))
    route = [(i - distance, i) for i in devices if i - distance in devices]
    return lax.ppermute(block, axis, route)


def xor_route(axis, bit):
    return [(i, i ^ (1 << bit)) for i in range(lax.axis_size(axis))]


def sum_over(block, axis, order):
    for bit in order:
        block = block + lax.ppermute(block, axis, xor_route(axis, bit))
    return block


def sum_scatter_blocks(held, axis):
    bits = lax.axis_size(axis).bit_length() - 1
    held = held.reshape((2,) * bits + held.shape[1:])
    for bit in range(bits):
        place = bits - 1 - bit
        kept = lax.index_in_dim(held, 0, place, keepdims=False)
        sent = lax.index_in_dim(held, 1, place, keepdims=False)
        held = kept + lax.ppermute(sent, axis, xor_route(axis, bit))
    return held


def windows(offsets, patch_side, width_cols):
    rows = offsets[:, 0]
    cols = offsets[:, 1]
    base = (rows // SUB) * SUB
    down = rows - base
    start = jnp.minimum((cols // LANE) * LANE, width_cols - patch_side - LANE)
    shift = cols - start
    return base, down, start, shift


def extract_kernel(base_ref, down_ref, start_ref, shift_ref, ext_ref, out_ref):
    s = pl.program_id(0)
    side = out_ref.shape[-1]
    high = side + SUB
    wide = side + LANE
    base = pl.multiple_of(base_ref[s], SUB)
    start = pl.multiple_of(start_ref[s], LANE)
    up = (high - down_ref[s]) % high
    left = (wide - shift_ref[s]) % wide
    for c in range(2):
        win = ext_ref[c, pl.ds(base, high), pl.ds(start, wide)]
        win = pltpu.roll(win, up, 0)
        win = pltpu.roll(win, left, 1)
        out_ref[0, c] = win[:side, :side]


def extract_patches(extended, base, down, start, shift, patch_side):
    slots = base.shape[0]
    grid_spec = pltpu.PrefetchScalarGridSpec(
        num_scalar_prefetch=4,
        grid=(slots,),
        in_specs=[pl.BlockSpec(extended.shape, lambda s, *_: (0, 0, 0))],
        out_specs=pl.BlockSpec((1, 2, patch_side, patch_side), lambda s, *_: (s, 0, 0, 0)),
    )
    return pl.pallas_call(
        extract_kernel,
        grid_spec=grid_spec,
        out_shape=jax.ShapeDtypeStruct((slots, 2, patch_side, patch_side), jnp.float32),
        compiler_params=pltpu.CompilerParams(vmem_limit_bytes=48 * 1024 * 1024),
    )(base, down, start, shift, extended)


def accumulate_kernel(base_ref, down_ref, shift_ref, place_ref, count_ref, terms_ref, out_ref, pad_ref):
    s = pl.program_id(0)
    side = terms_ref.shape[-1]
    high = side + SUB
    spans = place_ref.shape[1]

    @pl.when(s == 0)
    def _():
        out_ref[...] = jnp.zeros_like(out_ref)
        pad_ref[...] = jnp.zeros_like(pad_ref)

    @pl.when(s < count_ref[0])
    def _():
        base = pl.multiple_of(base_ref[s], SUB)
        down = down_ref[s]
        shift = shift_ref[s]
        for c in range(2):
            pad_ref[:side, :side] = terms_ref[0, c]
            term = pltpu.roll(pad_ref[...], down, 0)
            term = pltpu.roll(term, shift, 1)
            for k in range(spans):
                out_ref[place_ref[s, k], c, pl.ds(base, high), :] += term[:, k * LANE:(k + 1) * LANE]


def accumulate_terms(terms, base, down, shift, place, count, blocks, rows_out):
    slots, _, side, _ = terms.shape
    grid_spec = pltpu.PrefetchScalarGridSpec(
        num_scalar_prefetch=5,
        grid=(slots,),
        in_specs=[pl.BlockSpec((1, 2, side, side), lambda s, *_: (s, 0, 0, 0))],
        out_specs=pl.BlockSpec((blocks, 2, rows_out, LANE), lambda s, *_: (0, 0, 0, 0)),
        scratch_shapes=[pltpu.VMEM((side + SUB, side + LANE), jnp.float32)],
    )
    return pl.pallas_call(
        accumulate_kernel,
        grid_spec=grid_spec,
        out_shape=jax.ShapeDtypeStruct((blocks, 2, rows_out, LANE), jnp.float32),
        compiler_params=pltpu.CompilerParams(vmem_limit_bytes=48 * 1024 * 1024),
    )(base, down, shift, place, count, terms)


def fused_kernel(base_ref, down_ref, start_ref, shift_ref, place_ref, count_ref,
                 tile_ref, rim_ref, probe_ref, pattern_ref, fwd_ref, bwd_ref,
                 grad_ref, prb_ref, ext_ref, pad_ref, sems):
    s = pl.program_id(0)
    side = probe_ref.shape[-1]
    tile_rows = tile_ref.shape[1]
    high = side + SUB
    wide = side + LANE
    spans = place_ref.shape[1]

    @pl.when(s == 0)
    def _():
        own = pltpu.make_async_copy(tile_ref, ext_ref.at[:, :tile_rows, :], sems.at[0])
        rim = pltpu.make_async_copy(rim_ref, ext_ref.at[:, tile_rows:, :], sems.at[1])
        own.start()
        rim.start()
        grad_ref[...] = jnp.zeros_like(grad_ref)
        prb_ref[...] = jnp.zeros_like(prb_ref)
        pad_ref[...] = jnp.zeros_like(pad_ref)
        own.wait()
        rim.wait()

    @pl.when(s < count_ref[0])
    def _():
        base = pl.multiple_of(base_ref[s], SUB)
        start = pl.multiple_of(start_ref[s], LANE)
        down = down_ref[s]
        shift = shift_ref[s]
        up = (high - down) % high
        left = (wide - shift) % wide
        cut = []
        for c in range(2):
            win = ext_ref[c, pl.ds(base, high), pl.ds(start, wide)]
            win = pltpu.roll(win, up, 0)
            win = pltpu.roll(win, left, 1)
            cut.append(win[:side, :side])
        x_re, x_im = cut
        p_re = probe_ref[0]
        p_im = probe_ref[1]
        fwd = fwd_ref[...]
        bwd = bwd_ref[...]

        def dot(a, b):
            return jnp.dot(a, b, preferred_element_type=jnp.float32)

        wave = jnp.concatenate(
            [(p_re * x_re - p_im * x_im).astype(jnp.bfloat16),
             (p_re * x_im + p_im * x_re).astype(jnp.bfloat16)], axis=0)
        half = dot(fwd, wave).astype(jnp.bfloat16)
        far = dot(jnp.concatenate([half[:side], half[side:]], axis=1), bwd)
        far_re = far[:, :side]
        far_im = far[:, side:]
        excess = far_re * far_re + far_im * far_im - pattern_ref[0].astype(jnp.float32)
        back = jnp.concatenate(
            [(excess * far_re).astype(jnp.bfloat16), (excess * far_im).astype(jnp.bfloat16)],
            axis=0)
        inner = dot(bwd, back).astype(jnp.bfloat16)
        chi = dot(jnp.concatenate([inner[:side], inner[side:]], axis=1), fwd)
        chi_re = chi[:, :side]
        chi_im = chi[:, side:]
        prb_ref[0] += x_re * chi_re + x_im * chi_im
        prb_ref[1] += x_re * chi_im - x_im * chi_re
        terms = (p_re * chi_re + p_im * chi_im, p_re * chi_im - p_im * chi_re)
        for c in range(2):
            pad_ref[:side, :side] = terms[c]
            term = pltpu.roll(pad_ref[...], down, 0)
            term = pltpu.roll(term, shift, 1)
            for k in range(spans):
                grad_ref[place_ref[s, k], c, pl.ds(base, high), :] += term[:, k * LANE:(k + 1) * LANE]


def fused_step(tile, rim, probe, patterns, fwd, bwd, base, down, start, shift, place,
               count, blocks):
    slots, side, _ = patterns.shape
    rows_out = tile.shape[1] + rim.shape[1]
    whole2 = lambda s, *_: (0, 0)
    whole3 = lambda s, *_: (0, 0, 0)
    grid_spec = pltpu.PrefetchScalarGridSpec(
        num_scalar_prefetch=6,
        grid=(slots,),
        in_specs=[
            pl.BlockSpec(memory_space=pl.ANY),
            pl.BlockSpec(memory_space=pl.ANY),
            pl.BlockSpec(probe.shape, whole3),
            pl.BlockSpec((1, side, side), lambda s, *_: (s, 0, 0)),
            pl.BlockSpec(fwd.shape, whole2),
            pl.BlockSpec(bwd.shape, whole2),
        ],
        out_specs=[
            pl.BlockSpec((blocks, 2, rows_out, LANE), lambda s, *_: (0, 0, 0, 0)),
            pl.BlockSpec(probe.shape, whole3),
        ],
        scratch_shapes=[
            pltpu.VMEM((2, rows_out, tile.shape[2]), jnp.float32),
            pltpu.VMEM((side + SUB, side + LANE), jnp.float32),
            pltpu.SemaphoreType.DMA((2,)),
        ],
    )
    return pl.pallas_call(
        fused_kernel,
        grid_spec=grid_spec,
        out_shape=(
            jax.ShapeDtypeStruct((blocks, 2, rows_out, LANE), jnp.float32),
            jax.ShapeDtypeStruct(probe.shape, jnp.float32),
        ),
        compiler_params=pltpu.CompilerParams(vmem_limit_bytes=60 * 1024 * 1024),
    )(base, down, start, shift, place, count, tile, rim, probe, patterns, fwd, bwd)


def stacked_tables(cos_table, sin_table):
    fwd = jnp.concatenate(
        [jnp.concatenate([cos_table, sin_table], axis=1),
         jnp.concatenate([-sin_table, cos_table], axis=1)], axis=0)
    bwd = jnp.concatenate(
        [jnp.concatenate([cos_table, -sin_table], axis=1),
         jnp.concatenate([sin_table, cos_table], axis=1)], axis=0)
    return fwd, bwd


def make_tables(patch_side):
    index = jnp.arange(patch_side, dtype=jnp.int32)
    phase_int = index[:, None] * index[None, :] % patch_side
    phase = phase_int.astype(jnp.float32) * (2.0 * math.pi / patch_side)
    scale = 1.0 / math.sqrt(patch_side)
    return (
        (jnp.cos(phase) * scale).astype(jnp.bfloat16),
        (jnp.sin(phase) * scale).astype(jnp.bfloat16),
    )


def apply_left(table, field_part):
    return jnp.einsum("kn,bnm->bkm", table, field_part, preferred_element_type=jnp.float32)


def apply_right(field_part, table):
    return jnp.einsum("bkn,nm->bkm", field_part, table, preferred_element_type=jnp.float32)


def on_device(object_field, probes, patterns, offsets, counts):
    tile_rows = object_field.shape[1]
    width_cols = object_field.shape[2]
    patch_side = probes.shape[-1]
    slot_total = offsets.shape[0]
    top_rows = object_field[:, :patch_side, :]
    rim_rows = from_behind(top_rows, "region", -1)
    base, down, start, shift = windows(offsets, patch_side, width_cols)
    cos_table, sin_table = make_tables(patch_side)
    blocks = lax.axis_size("wave")
    spans = (patch_side + LANE) // LANE
    first = start // LANE
    place = jnp.bitwise_xor(
        first[:, None] + jnp.arange(spans, dtype=jnp.int32)[None, :], lax.axis_index("wave")
    ).astype(jnp.int32)
    fwd, bwd = stacked_tables(cos_table, sin_table)
    grad_ext, probe_part = fused_step(
        object_field, rim_rows, probes[0], patterns[0], fwd, bwd, base, down, start, shift,
        place, counts, blocks,
    )
    probe_total = sum_over(probe_part, "region", (3, 4, 0, 1, 2))
    arrived = from_behind(grad_ext[:, :, tile_rows:, :], "region", 1)
    tile_grad = grad_ext[:, :, :tile_rows, :] + jnp.pad(
        arrived, ((0, 0), (0, 0), (0, tile_rows - patch_side), (0, 0))
    )
    object_out = sum_scatter_blocks(tile_grad, "wave")
    return (object_out, probe_total[None])


def solution(mesh):
    in_specs = (
        P(None, "region", None),
        P("wave", None, None, None),
        P("wave", "region", None, None),
        P("region", None),
        P("region"),
    )
    out_specs = (P(None, "region", "wave"), P("wave", None, None, None))
    return jax.shard_map(
        on_device, mesh=mesh, in_specs=in_specs, out_specs=out_specs, check_vma=False
    )
```

```python
import math

import jax
import jax.numpy as jnp
from jax import lax
from jax.experimental import pallas as pl
from jax.experimental.pallas import tpu as pltpu
from jax.sharding import PartitionSpec as P

SUB = 8
LANE = 128


def from_behind(block, axis, distance):
    devices = range(lax.axis_size(axis))
    route = [(i - distance, i) for i in devices if i - distance in devices]
    return lax.ppermute(block, axis, route)


def xor_route(axis, bit):
    return [(i, i ^ (1 << bit)) for i in range(lax.axis_size(axis))]


def sum_over(block, axis, order):
    for bit in order:
        block = block + lax.ppermute(block, axis, xor_route(axis, bit))
    return block


def sum_scatter_blocks(held, axis, other):
    count = lax.axis_size(axis)
    others = lax.axis_size(other)
    bits = count.bit_length() - 1
    odd = lax.axis_index(other) % 2 == 1
    held = held.reshape((2,) * bits + held.shape[1:])
    for bit in range(bits):
        place = bits - 1 - bit
        kept = lax.index_in_dim(held, 0, place, keepdims=False)
        sent = lax.index_in_dim(held, 1, place, keepdims=False)
        if bit == 0 and bits >= 2:
            route = [
                (w * others + r, (w ^ (1 if r % 2 == 0 else 3)) * others + r)
                for w in range(count)
                for r in range(others)
            ]
            got = lax.ppermute(sent, (axis, other), route)
            got = jnp.where(odd, jnp.flip(got, axis=place - 1), got)
        else:
            got = lax.ppermute(sent, axis, xor_route(axis, bit))
        held = kept + got
    return held


def windows(offsets, patch_side, width_cols):
    rows = offsets[:, 0]
    cols = offsets[:, 1]
    base = (rows // SUB) * SUB
    down = rows - base
    start = jnp.minimum((cols // LANE) * LANE, width_cols - patch_side - LANE)
    shift = cols - start
    return base, down, start, shift


def extract_kernel(base_ref, down_ref, start_ref, shift_ref, ext_ref, out_ref):
    s = pl.program_id(0)
    side = out_ref.shape[-1]
    high = side + SUB
    wide = side + LANE
    base = pl.multiple_of(base_ref[s], SUB)
    start = pl.multiple_of(start_ref[s], LANE)
    up = (high - down_ref[s]) % high
    left = (wide - shift_ref[s]) % wide
    for c in range(2):
        win = ext_ref[c, pl.ds(base, high), pl.ds(start, wide)]
        win = pltpu.roll(win, up, 0)
        win = pltpu.roll(win, left, 1)
        out_ref[0, c] = win[:side, :side]


def extract_patches(extended, base, down, start, shift, patch_side):
    slots = base.shape[0]
    grid_spec = pltpu.PrefetchScalarGridSpec(
        num_scalar_prefetch=4,
        grid=(slots,),
        in_specs=[pl.BlockSpec(extended.shape, lambda s, *_: (0, 0, 0))],
        out_specs=pl.BlockSpec((1, 2, patch_side, patch_side), lambda s, *_: (s, 0, 0, 0)),
    )
    return pl.pallas_call(
        extract_kernel,
        grid_spec=grid_spec,
        out_shape=jax.ShapeDtypeStruct((slots, 2, patch_side, patch_side), jnp.float32),
        compiler_params=pltpu.CompilerParams(vmem_limit_bytes=48 * 1024 * 1024),
    )(base, down, start, shift, extended)


def accumulate_kernel(base_ref, down_ref, shift_ref, place_ref, count_ref, terms_ref, out_ref, pad_ref):
    s = pl.program_id(0)
    side = terms_ref.shape[-1]
    high = side + SUB
    spans = place_ref.shape[1]

    @pl.when(s == 0)
    def _():
        out_ref[...] = jnp.zeros_like(out_ref)
        pad_ref[...] = jnp.zeros_like(pad_ref)

    @pl.when(s < count_ref[0])
    def _():
        base = pl.multiple_of(base_ref[s], SUB)
        down = down_ref[s]
        shift = shift_ref[s]
        for c in range(2):
            pad_ref[:side, :side] = terms_ref[0, c]
            term = pltpu.roll(pad_ref[...], down, 0)
            term = pltpu.roll(term, shift, 1)
            for k in range(spans):
                out_ref[place_ref[s, k], c, pl.ds(base, high), :] += term[:, k * LANE:(k + 1) * LANE]


def accumulate_terms(terms, base, down, shift, place, count, blocks, rows_out):
    slots, _, side, _ = terms.shape
    grid_spec = pltpu.PrefetchScalarGridSpec(
        num_scalar_prefetch=5,
        grid=(slots,),
        in_specs=[pl.BlockSpec((1, 2, side, side), lambda s, *_: (s, 0, 0, 0))],
        out_specs=pl.BlockSpec((blocks, 2, rows_out, LANE), lambda s, *_: (0, 0, 0, 0)),
        scratch_shapes=[pltpu.VMEM((side + SUB, side + LANE), jnp.float32)],
    )
    return pl.pallas_call(
        accumulate_kernel,
        grid_spec=grid_spec,
        out_shape=jax.ShapeDtypeStruct((blocks, 2, rows_out, LANE), jnp.float32),
        compiler_params=pltpu.CompilerParams(vmem_limit_bytes=48 * 1024 * 1024),
    )(base, down, shift, place, count, terms)


def fused_kernel(base_ref, down_ref, start_ref, shift_ref, place_ref, count_ref,
                 tile_ref, rim_ref, probe_ref, pattern_ref, fwd_ref, bwd_ref,
                 grad_ref, prb_ref, ext_ref, pad_ref, sems):
    s = pl.program_id(0)
    side = probe_ref.shape[-1]
    tile_rows = tile_ref.shape[1]
    high = side + SUB
    wide = side + LANE
    spans = place_ref.shape[1]

    @pl.when(s == 0)
    def _():
        own = pltpu.make_async_copy(tile_ref, ext_ref.at[:, :tile_rows, :], sems.at[0])
        rim = pltpu.make_async_copy(rim_ref, ext_ref.at[:, tile_rows:, :], sems.at[1])
        own.start()
        rim.start()
        grad_ref[...] = jnp.zeros_like(grad_ref)
        prb_ref[...] = jnp.zeros_like(prb_ref)
        pad_ref[...] = jnp.zeros_like(pad_ref)
        own.wait()
        rim.wait()

    @pl.when(s < count_ref[0])
    def _():
        base = pl.multiple_of(base_ref[s], SUB)
        start = pl.multiple_of(start_ref[s], LANE)
        down = down_ref[s]
        shift = shift_ref[s]
        up = (high - down) % high
        left = (wide - shift) % wide
        cut = []
        for c in range(2):
            win = ext_ref[c, pl.ds(base, high), pl.ds(start, wide)]
            win = pltpu.roll(win, up, 0)
            win = pltpu.roll(win, left, 1)
            cut.append(win[:side, :side])
        x_re, x_im = cut
        p_re = probe_ref[0]
        p_im = probe_ref[1]
        fwd = fwd_ref[...]
        bwd = bwd_ref[...]

        def dot(a, b):
            return jnp.dot(a, b, preferred_element_type=jnp.float32)

        wave = jnp.concatenate(
            [(p_re * x_re - p_im * x_im).astype(jnp.bfloat16),
             (p_re * x_im + p_im * x_re).astype(jnp.bfloat16)], axis=0)
        half = dot(fwd, wave).astype(jnp.bfloat16)
        far = dot(jnp.concatenate([half[:side], half[side:]], axis=1), bwd)
        far_re = far[:, :side]
        far_im = far[:, side:]
        excess = far_re * far_re + far_im * far_im - pattern_ref[0].astype(jnp.float32)
        back = jnp.concatenate(
            [(excess * far_re).astype(jnp.bfloat16), (excess * far_im).astype(jnp.bfloat16)],
            axis=0)
        inner = dot(bwd, back).astype(jnp.bfloat16)
        chi = dot(jnp.concatenate([inner[:side], inner[side:]], axis=1), fwd)
        chi_re = chi[:, :side]
        chi_im = chi[:, side:]
        prb_ref[0] += x_re * chi_re + x_im * chi_im
        prb_ref[1] += x_re * chi_im - x_im * chi_re
        terms = (p_re * chi_re + p_im * chi_im, p_re * chi_im - p_im * chi_re)
        for c in range(2):
            pad_ref[:side, :side] = terms[c]
            term = pltpu.roll(pad_ref[...], down, 0)
            term = pltpu.roll(term, shift, 1)
            for k in range(spans):
                grad_ref[place_ref[s, k], c, pl.ds(base, high), :] += term[:, k * LANE:(k + 1) * LANE]


def fused_step(tile, rim, probe, patterns, fwd, bwd, base, down, start, shift, place,
               count, blocks):
    slots, side, _ = patterns.shape
    rows_out = tile.shape[1] + rim.shape[1]
    whole2 = lambda s, *_: (0, 0)
    whole3 = lambda s, *_: (0, 0, 0)
    grid_spec = pltpu.PrefetchScalarGridSpec(
        num_scalar_prefetch=6,
        grid=(slots,),
        in_specs=[
            pl.BlockSpec(memory_space=pl.ANY),
            pl.BlockSpec(memory_space=pl.ANY),
            pl.BlockSpec(probe.shape, whole3),
            pl.BlockSpec((1, side, side), lambda s, *_: (s, 0, 0)),
            pl.BlockSpec(fwd.shape, whole2),
            pl.BlockSpec(bwd.shape, whole2),
        ],
        out_specs=[
            pl.BlockSpec((blocks, 2, rows_out, LANE), lambda s, *_: (0, 0, 0, 0)),
            pl.BlockSpec(probe.shape, whole3),
        ],
        scratch_shapes=[
            pltpu.VMEM((2, rows_out, tile.shape[2]), jnp.float32),
            pltpu.VMEM((side + SUB, side + LANE), jnp.float32),
            pltpu.SemaphoreType.DMA((2,)),
        ],
    )
    return pl.pallas_call(
        fused_kernel,
        grid_spec=grid_spec,
        out_shape=(
            jax.ShapeDtypeStruct((blocks, 2, rows_out, LANE), jnp.float32),
            jax.ShapeDtypeStruct(probe.shape, jnp.float32),
        ),
        compiler_params=pltpu.CompilerParams(vmem_limit_bytes=60 * 1024 * 1024),
    )(base, down, start, shift, place, count, tile, rim, probe, patterns, fwd, bwd)


def stacked_tables(cos_table, sin_table):
    fwd = jnp.concatenate(
        [jnp.concatenate([cos_table, sin_table], axis=1),
         jnp.concatenate([-sin_table, cos_table], axis=1)], axis=0)
    bwd = jnp.concatenate(
        [jnp.concatenate([cos_table, -sin_table], axis=1),
         jnp.concatenate([sin_table, cos_table], axis=1)], axis=0)
    return fwd, bwd


def make_tables(patch_side):
    index = jnp.arange(patch_side, dtype=jnp.int32)
    phase_int = index[:, None] * index[None, :] % patch_side
    phase = phase_int.astype(jnp.float32) * (2.0 * math.pi / patch_side)
    scale = 1.0 / math.sqrt(patch_side)
    return (
        (jnp.cos(phase) * scale).astype(jnp.bfloat16),
        (jnp.sin(phase) * scale).astype(jnp.bfloat16),
    )


def apply_left(table, field_part):
    return jnp.einsum("kn,bnm->bkm", table, field_part, preferred_element_type=jnp.float32)


def apply_right(field_part, table):
    return jnp.einsum("bkn,nm->bkm", field_part, table, preferred_element_type=jnp.float32)


def on_device(object_field, probes, patterns, offsets, counts):
    tile_rows = object_field.shape[1]
    width_cols = object_field.shape[2]
    patch_side = probes.shape[-1]
    slot_total = offsets.shape[0]
    top_rows = object_field[:, :patch_side, :]
    rim_rows = from_behind(top_rows, "region", -1)
    base, down, start, shift = windows(offsets, patch_side, width_cols)
    cos_table, sin_table = make_tables(patch_side)
    blocks = lax.axis_size("wave")
    spans = (patch_side + LANE) // LANE
    first = start // LANE
    place = jnp.bitwise_xor(
        first[:, None] + jnp.arange(spans, dtype=jnp.int32)[None, :], lax.axis_index("wave")
    ).astype(jnp.int32)
    fwd, bwd = stacked_tables(cos_table, sin_table)
    grad_ext, probe_part = fused_step(
        object_field, rim_rows, probes[0], patterns[0], fwd, bwd, base, down, start, shift,
        place, counts, blocks,
    )
    probe_total = sum_over(probe_part, "region", (3, 4, 0, 1, 2))
    arrived = from_behind(grad_ext[:, :, tile_rows:, :], "region", 1)
    tile_grad = grad_ext[:, :, :tile_rows, :] + jnp.pad(
        arrived, ((0, 0), (0, 0), (0, tile_rows - patch_side), (0, 0))
    )
    object_out = sum_scatter_blocks(tile_grad, "wave", "region")
    return (object_out, probe_total[None])


def solution(mesh):
    in_specs = (
        P(None, "region", None),
        P("wave", None, None, None),
        P("wave", "region", None, None),
        P("region", None),
        P("region"),
    )
    out_specs = (P(None, "region", "wave"), P("wave", None, None, None))
    return jax.shard_map(
        on_device, mesh=mesh, in_specs=in_specs, out_specs=out_specs, check_vma=False
    )
```
